256 devices in a mesh: dp: 8 (over z), expert: 32 (over y, x, core).
Axes of the slice: x: 4, y: 4, z: 8, core: 2. Of those that a mesh axis runs over, the one named last changes fastest.
Arguments:
- hidden_in: bfloat16 [16384, 2560], P(('dp', 'expert')), may hold values from -420 to 420
- norm_gain: float32 [2560], replicated, may hold values from 0.25 to 1.75
- expert_ids: int32 [16384, 6], P(('dp', 'expert')), may hold values from 0 to 63, all different within a row; in each aligned block of 64 rows (0 to 63, 64 to 127, ...) at most 7 rows name the same one
- gate_weights: bfloat16 [16384, 6], P(('dp', 'expert')), may hold values from 0.049804688 to 0.5
- expert_slot: int32 [64], replicated, may hold values from 0 to 63, each once
- w_in: bfloat16 [64, 2560, 3072], P('expert', None, 'dp'), may hold values from -0.125 to 0.125
- w_down: bfloat16 [64, 1536, 2560], P('expert', 'dp'), may hold values from -0.15625 to 0.15625
- shared_in: bfloat16 [2560, 6144], P(None, 'dp'), may hold values from -0.125 to 0.125
- shared_down: bfloat16 [3072, 2560], P('dp'), may hold values from -0.109375 to 0.109375
Outputs:
- mixed: bfloat16 [16384, 2560], P(('dp', 'expert'))
The draws below stay inside these ranges and needn't reach their ends.
Inputs may be any that keep to these rules, and one draw needn't show every extreme that they name: `expert_ids`: each token names 6 different experts; among the tokens of one device no expert is named by more than 7. `expert_slot`: each slot holds exactly one expert.
All inputs are finite; a program needn't handle non-finite values.
Results may differ from the reference program's by a relative error of at most 0.0085.
Values may be sent and summed in bfloat16 or wider, within the bound.
No kernel may reach another device: no remote copies, remote signals or barrier semaphores. Data moves between devices by JAX's collectives and lax.ppermute only.
A program may use at most 192 MiB of HBM per device.

```python
import math
import jax
import jax.numpy as jnp
import numpy as np
from jax import lax

D = 2560
FF_E = 1536
SH_FF = 3072
TOP = 6
TOK_DEV = 64
EXPERTS = 64
CAP = 7
TOKENS = 16384
N_DP = 8


def draw_hidden_in(key, part):
    base_key = jax.random.fold_in(key, 11)
    subkeys = jax.random.split(base_key, 3)
    row_scale = jnp.exp(jax.random.uniform(subkeys[1], (TOKENS, 1), jnp.float32) * math.log(10.0))
    col_scale = jnp.exp(jax.random.uniform(subkeys[2], (1, D), jnp.float32) * math.log(10.0))
    values = jnp.clip(jax.random.normal(subkeys[0], (TOKENS, D), jnp.float32), -4.0, 4.0)
    return (values * row_scale * col_scale).astype(jnp.bfloat16)


def levels(stream_key, shape, shards, least, top_value):
    level, own = 1.0, jax.random.fold_in(stream_key, 6)
    for dim, shards_of in shards:
        heights = jnp.exp(jax.random.uniform(jax.random.fold_in(own, dim), (shards_of,), jnp.float32, least / len(shards), top_value / len(shards)))
        level = level * jnp.repeat(heights, shape[dim] // shards_of).reshape([-1 if axis == dim else 1 for axis in range(len(shape))])
    return level


def shared_out(rng, own, number, rows, count, top, most, lean):
    order = jax.random.permutation(rng, count)
    crowded, usual = shares(count, rows * top, most, lean, True), shares(count, rows * top, most, lean, False)
    places = jnp.arange(count)

    def named(sizes, turn):
        used = int((sizes > 0).sum())
        fixed = max(1, used // 4)
        passed = fixed + (places - fixed + turn * (used - fixed)) % max(1, count - fixed)
        return jnp.zeros((count,), jnp.int32).at[order[jnp.where(places < fixed, places, passed)]].set(jnp.asarray(sizes, jnp.int32))

    sizes = jnp.where(number % 4 == 0, named(crowded, number // 4), named(usual, number - number // 4 - 1))
    mixed = jax.random.permutation(jax.random.fold_in(own, 3), count)
    donor, receiver = mixed[0:count // 2 * 2:2], mixed[1:count // 2 * 2:2]
    room = jnp.minimum(sizes[donor] - 1, most - sizes[receiver]) // 2
    room = jnp.where((donor == order[0]) | (receiver == order[0]) | (sizes[receiver] == 0), 0, jnp.maximum(room, 0))
    passed = jax.random.randint(jax.random.fold_in(own, 4), (count // 2,), 0, 1 << 20) % (room + 1)
    sizes = sizes.at[donor].add(-passed).at[receiver].add(passed)
    items = jnp.searchsorted(jnp.cumsum(sizes), jnp.arange(rows * top), side="right").astype(jnp.int32)
    table = items.reshape(top, rows).T
    table = table[jax.random.permutation(jax.random.fold_in(own, 1), rows)]
    turn = jax.random.randint(jax.random.fold_in(own, 2), (rows, 1), 0, top)
    return jnp.take_along_axis(table, (jnp.arange(top)[None, :] + turn) % top, axis=1)


def shares(number_of, total, bound, lean, full):
    weights = [(1 << 20) // math.isqrt(grade ** lean) + 1 for grade in range(1, number_of + 1)]
    largest = bound if full else min(bound, max(-(-total // number_of), total * weights[0] // sum(weights)))
    least = 1 if total - largest >= number_of - 1 else 0
    counts, rest = [largest] + [least] * (number_of - 1), total - largest - least * (number_of - 1)
    while rest > 0:
        movable = [i for i in range(1, number_of) if counts[i] < largest] or [i for i in range(1, number_of) if counts[i] < bound]
        whole, left = sum([weights[i] for i in movable]), rest
        for i in movable:
            more = min(bound - counts[i], max(1, left * weights[i] // whole), rest)
            counts[i] = counts[i] + more
            rest = rest - more
    return np.array(counts)


def gaussian(key, dims, deviation, most, cuts=(), held_as=jnp.bfloat16):
    array = deviation * jax.random.normal(key, dims, jnp.float32)
    if cuts:
        array = array * levels(key, dims, cuts, -0.22, 0.18)
    return jnp.clip(array, -most, most).astype(held_as)


def setup_inputs(seed: int = 0) -> dict:
    key_of = jax.random.split(jax.random.key(seed), 10)
    hidden_in = draw_hidden_in(jax.random.fold_in(key_of[9], 71), 0)
    norm_gain = jnp.clip(1.0 + 0.15 * jax.random.normal(key_of[1], (D,), jnp.float32), 0.25, 1.75)
    expert_ids_keys = jax.random.split(jax.random.fold_in(key_of[2], 1), TOKENS // TOK_DEV)
    expert_ids_turns = jax.random.permutation(jax.random.fold_in(key_of[2], 3), TOKENS // TOK_DEV)
    expert_ids = jax.vmap(lambda own, number: shared_out(jax.random.fold_in(key_of[2], 2), own, number, TOK_DEV, EXPERTS, TOP, CAP, 2))(expert_ids_keys, expert_ids_turns).reshape((TOKENS, TOP))
    gate_weights = jnp.clip(jnp.exp(math.log(0.5) - 2.306499 * jax.random.uniform(key_of[3], (TOKENS, TOP), jnp.float32) ** levels(key_of[3], (TOKENS, TOP), ((0, 256),), -0.2, 0.2)), 0.049804688, 0.5).astype(jnp.bfloat16)
    expert_slot = jax.random.permutation(key_of[4], EXPERTS).astype(jnp.int32)
    w_in = gaussian(key_of[5], (EXPERTS, D, 2 * FF_E), D ** -0.5, 0.125, ((0, 32), (2, 8)))
    w_down = gaussian(key_of[6], (EXPERTS, FF_E, D), FF_E ** -0.5, 0.15625, ((0, 32), (1, 8)))
    shared_in = gaussian(key_of[7], (D, 2 * SH_FF), D ** -0.5, 0.125, ((1, 8),))
    shared_down = gaussian(key_of[8], (SH_FF, D), SH_FF ** -0.5, 0.109375, ((0, 8),))
    return {"hidden_in": hidden_in, "norm_gain": norm_gain, "expert_ids": expert_ids, "gate_weights": gate_weights, "expert_slot": expert_slot, "w_in": w_in, "w_down": w_down, "shared_in": shared_in, "shared_down": shared_down}


epsilon = 1e-06

def normalize(hidden, gain):
    widened = hidden.astype(jnp.float32)
    mean_square = lax.optimization_barrier(jnp.mean(widened * widened, axis=-1, keepdims=True))
    return (widened * lax.rsqrt(mean_square + epsilon) * gain).astype(jnp.bfloat16)

def slice_parts(rows, weight_in, weight_down):
    slice_width = weight_down.shape[0] // N_DP
    gate_up = jnp.dot(rows, weight_in, preferred_element_type=jnp.float32)
    gate_up = gate_up.reshape(rows.shape[0], N_DP, 2, slice_width)
    activated = (jax.nn.silu(gate_up[:, :, 0]) * gate_up[:, :, 1]).astype(jnp.bfloat16)
    accumulated = jnp.zeros((rows.shape[0], weight_down.shape[1]), jnp.float32)
    for piece in range(N_DP):
        partial_value = jnp.dot(activated[:, piece], weight_down[piece * slice_width:(piece + 1) * slice_width], preferred_element_type=jnp.float32).astype(jnp.bfloat16)
        accumulated = accumulated + lax.optimization_barrier(partial_value).astype(jnp.float32)
    return accumulated

def reference(hidden_in, norm_gain, expert_ids, gate_weights, expert_slot, w_in, w_down, shared_in, shared_down):
    normed = normalize(hidden_in, norm_gain)
    block_count = TOKENS // TOK_DEV
    block_routes = expert_ids.reshape(block_count, TOK_DEV * TOP)
    onehot = (block_routes[:, :, None] == jnp.arange(EXPERTS, dtype=jnp.int32)[None, None, :]).astype(jnp.int32)
    slot_rank = lax.optimization_barrier(jnp.sum(jnp.cumsum(onehot, axis=1) * onehot, axis=2)) - 1
    position = (jnp.arange(block_count, dtype=jnp.int32)[:, None] * CAP + slot_rank).reshape(-1).astype(jnp.int32)
    source_row = jnp.repeat(jnp.arange(TOKENS, dtype=jnp.int32), TOP)
    flat_routes = expert_ids.reshape(-1).astype(jnp.int32)
    row_table = jnp.full((EXPERTS, block_count * CAP), TOKENS, jnp.int32).at[flat_routes, position].set(source_row)
    padded = jnp.concatenate([normed, jnp.zeros((1, D), jnp.bfloat16)], axis=0)

    def one_expert(expert):
        rows = padded[row_table[expert]]
        slot_index = expert_slot[expert]
        return slice_parts(rows, w_in[slot_index], w_down[slot_index])
    results = lax.map(one_expert, jnp.arange(EXPERTS, dtype=jnp.int32))
    picked = results[flat_routes, position].reshape(TOKENS, TOP, D)
    routed = lax.optimization_barrier(jnp.sum(gate_weights.astype(jnp.float32)[:, :, None] * picked, axis=1))
    shared = slice_parts(normed, shared_in, shared_down)
    return (routed + shared).astype(jnp.bfloat16)
```

```python
import jax
import jax.numpy as jnp
from jax import lax
from jax.sharding import PartitionSpec as P

epsilon = 1e-06


def normalize(hidden, gain):
    widened = hidden.astype(jnp.float32)
    mean_square = jnp.mean(widened * widened, axis=-1, keepdims=True)
    return (widened * lax.rsqrt(mean_square + epsilon) * gain).astype(jnp.bfloat16)


def on_device(
    hidden_in,
    norm_gain,
    expert_ids,
    gate_weights,
    expert_slot,
    w_in,
    w_down,
    shared_in,
    shared_down,
):
    groups = lax.axis_size("dp")
    columns = lax.axis_size("expert")
    local_experts = w_in.shape[0]
    experts = local_experts * columns
    token_count = hidden_in.shape[0]
    top_count = expert_ids.shape[1]
    capacity = max(2, token_count * top_count * 7 // (6 * experts))
    row_total = groups * token_count
    normed = normalize(hidden_in, norm_gain)
    gathered, all_routes, all_gates = (
        lax.all_gather(normed, "dp", axis=0, tiled=True),
        lax.all_gather(expert_ids, "dp", axis=0, tiled=True),
        lax.all_gather(gate_weights, "dp", axis=0, tiled=True),
    )
    shared_width = shared_down.shape[0]
    shared_both = jnp.dot(gathered, shared_in, preferred_element_type=jnp.float32)
    shared_act = (
        jax.nn.silu(shared_both[:, :shared_width]) * shared_both[:, shared_width:]
    ).astype(jnp.bfloat16)
    shared_part = jnp.dot(shared_act, shared_down, preferred_element_type=jnp.float32).astype(
        jnp.bfloat16
    )
    block_routes = all_routes.reshape(groups, token_count * top_count)
    onehot = block_routes[:, :, None] == jnp.arange(experts, dtype=jnp.int32)[None, None, :]
    onehot_int = onehot.astype(jnp.int32)
    slot_rank = jnp.sum(jnp.cumsum(onehot_int, axis=1) * onehot_int, axis=2) - 1
    slot_of = jnp.sum(jnp.where(onehot, expert_slot[None, None, :], 0), axis=2)
    dest_col = slot_of // local_experts
    local_of = slot_of % local_experts
    group_of = jnp.arange(groups, dtype=jnp.int32)[:, None]
    position = ((dest_col * groups + group_of) * capacity + slot_rank).reshape(row_total, top_count)
    local_of = local_of.reshape(row_total, top_count)
    buffer_rows = columns * groups * capacity
    row_iota = jnp.arange(buffer_rows, dtype=jnp.int32)[None, None, :]
    slice_width = w_down.shape[1]
    routed = shared_part.astype(jnp.float32)
    for local in range(local_experts):
        hit = (position[:, :, None] == row_iota) & (local_of[:, :, None] == local)
        dispatch = jnp.any(hit, axis=1).astype(jnp.bfloat16)
        combine = jnp.sum(
            jnp.where(hit, all_gates[:, :, None], jnp.zeros((), jnp.bfloat16)), axis=1
        ).astype(jnp.bfloat16)
        outgoing = lax.dot_general(
            dispatch, gathered, (((0,), (0,)), ((), ())), preferred_element_type=jnp.float32
        ).astype(jnp.bfloat16)
        received = lax.all_to_all(outgoing, "expert", 0, 0, tiled=True)
        gate_up = jnp.dot(received, w_in[local], preferred_element_type=jnp.float32)
        activated = (
            jax.nn.silu(gate_up[:, :slice_width]) * gate_up[:, slice_width:]
        ).astype(jnp.bfloat16)
        partial_value = jnp.dot(activated, w_down[local], preferred_element_type=jnp.float32).astype(
            jnp.bfloat16
        )
        returned = lax.all_to_all(partial_value, "expert", 0, 0, tiled=True)
        routed = routed + jnp.dot(combine, returned, preferred_element_type=jnp.float32)
    mixed = lax.psum_scatter(routed, "dp", scatter_dimension=0, tiled=True)
    return mixed.astype(jnp.bfloat16)


def solution(mesh):
    return jax.shard_map(
        on_device,
        mesh=mesh,
        in_specs=(
            P(("dp", "expert"), None),
            P(),
            P(("dp", "expert"), None),
            P(("dp", "expert"), None),
            P(),
            P("expert", None, "dp"),
            P("expert", "dp", None),
            P(None, "dp"),
            P("dp", None),
        ),
        out_specs=P(("dp", "expert"), None),
        check_vma=False,
    )
```

```python
import jax
import jax.numpy as jnp
from jax import lax
from jax.sharding import PartitionSpec as P

epsilon = 1e-06


def normalize(hidden, gain):
    widened = hidden.astype(jnp.float32)
    mean_square = jnp.mean(widened * widened, axis=-1, keepdims=True)
    return (widened * lax.rsqrt(mean_square + epsilon) * gain).astype(jnp.bfloat16)


def on_device(
    hidden_in,
    norm_gain,
    expert_ids,
    gate_weights,
    expert_slot,
    w_in,
    w_down,
    shared_in,
    shared_down,
):
    groups = lax.axis_size("dp")
    columns = lax.axis_size("expert")
    local_experts = w_in.shape[0]
    experts = local_experts * columns
    token_count = hidden_in.shape[0]
    top_count = expert_ids.shape[1]
    capacity = max(2, token_count * top_count * 7 // (6 * experts))
    row_total = groups * token_count
    normed = normalize(hidden_in, norm_gain)
    meta = jnp.concatenate([expert_ids.astype(jnp.bfloat16), gate_weights], axis=1)
    gathered = lax.all_gather(normed, "dp", axis=0, tiled=True)
    all_meta = lax.all_gather(meta, "dp", axis=0, tiled=True)
    all_routes = all_meta[:, :top_count].astype(jnp.int32)
    all_gates = all_meta[:, top_count:]
    shared_width = shared_down.shape[0]
    shared_both = jnp.dot(gathered, shared_in, preferred_element_type=jnp.float32)
    shared_act = (
        jax.nn.silu(shared_both[:, :shared_width]) * shared_both[:, shared_width:]
    ).astype(jnp.bfloat16)
    shared_part = jnp.dot(shared_act, shared_down, preferred_element_type=jnp.float32).astype(
        jnp.bfloat16
    )
    slice_width = w_down.shape[1]

    def routes_of(routes, block_count):
        block_routes = routes.reshape(block_count, token_count * top_count)
        onehot = block_routes[:, :, None] == jnp.arange(experts, dtype=jnp.int32)[None, None, :]
        onehot_int = onehot.astype(jnp.int32)
        slot_rank = jnp.sum(jnp.cumsum(onehot_int, axis=1) * onehot_int, axis=2) - 1
        slot_of = jnp.sum(jnp.where(onehot, expert_slot[None, None, :], 0), axis=2)
        return slot_of // local_experts, slot_of % local_experts, slot_rank

    def expert_block(rows, local):
        gate_up = jnp.dot(rows, w_in[local], preferred_element_type=jnp.float32)
        activated = (
            jax.nn.silu(gate_up[:, :slice_width]) * gate_up[:, slice_width:]
        ).astype(jnp.bfloat16)
        return jnp.dot(activated, w_down[local], preferred_element_type=jnp.float32).astype(
            jnp.bfloat16
        )

    def one_hots(position, local_of, gates, local, buffer_rows):
        row_iota = jnp.arange(buffer_rows, dtype=jnp.int32)[None, None, :]
        hit = (position[:, :, None] == row_iota) & (local_of[:, :, None] == local)
        dispatch = jnp.any(hit, axis=1).astype(jnp.bfloat16)
        combine = jnp.sum(
            jnp.where(hit, gates[:, :, None], jnp.zeros((), jnp.bfloat16)), axis=1
        ).astype(jnp.bfloat16)
        return dispatch, combine

    dest_col, local_of, slot_rank = routes_of(all_routes, groups)
    group_of = jnp.arange(groups, dtype=jnp.int32)[:, None]
    position = ((dest_col * groups + group_of) * capacity + slot_rank).reshape(row_total, top_count)
    local_of = local_of.reshape(row_total, top_count)
    routed = shared_part.astype(jnp.float32)
    for local in range(local_experts - 1):
        dispatch, combine = one_hots(position, local_of, all_gates, local, columns * groups * capacity)
        outgoing = lax.dot_general(
            dispatch, gathered, (((0,), (0,)), ((), ())), preferred_element_type=jnp.float32
        ).astype(jnp.bfloat16)
        received = lax.all_to_all(outgoing, "expert", 0, 0, tiled=True)
        returned = lax.all_to_all(expert_block(received, local), "expert", 0, 0, tiled=True)
        routed = routed + jnp.dot(combine, returned, preferred_element_type=jnp.float32)
    last = local_experts - 1
    own_col, own_local, own_rank = routes_of(expert_ids, 1)
    own_position = (own_col * capacity + own_rank).reshape(token_count, top_count)
    own_local = own_local.reshape(token_count, top_count)
    dispatch, combine = one_hots(own_position, own_local, gate_weights, last, columns * capacity)
    outgoing = lax.dot_general(
        dispatch, normed, (((0,), (0,)), ((), ())), preferred_element_type=jnp.float32
    ).astype(jnp.bfloat16)
    received = lax.all_to_all(outgoing, "expert", 0, 0, tiled=True)
    spread = lax.all_gather(received, "dp", axis=0, tiled=True)
    summed = lax.psum_scatter(expert_block(spread, last), "dp", scatter_dimension=0, tiled=True)
    returned = lax.all_to_all(summed, "expert", 0, 0, tiled=True)
    own_routed = jnp.dot(combine, returned, preferred_element_type=jnp.float32)
    mixed = lax.psum_scatter(routed, "dp", scatter_dimension=0, tiled=True) + own_routed
    return mixed.astype(jnp.bfloat16)


def solution(mesh):
    return jax.shard_map(
        on_device,
        mesh=mesh,
        in_specs=(
            P(("dp", "expert"), None),
            P(),
            P(("dp", "expert"), None),
            P(("dp", "expert"), None),
            P(),
            P("expert", None, "dp"),
            P("expert", "dp", None),
            P(None, "dp"),
            P("dp", None),
        ),
        out_specs=P(("dp", "expert"), None),
        check_vma=False,
    )
```

```python
import jax
import jax.numpy as jnp
from jax import lax
from jax.sharding import PartitionSpec as P

epsilon = 1e-06


def normalize(hidden, gain):
    widened = hidden.astype(jnp.float32)
    mean_square = jnp.mean(widened * widened, axis=-1, keepdims=True)
    return (widened * lax.rsqrt(mean_square + epsilon) * gain).astype(jnp.bfloat16)


def on_device(
    hidden_in,
    norm_gain,
    expert_ids,
    gate_weights,
    expert_slot,
    w_in,
    w_down,
    shared_in,
    shared_down,
):
    groups = lax.axis_size("dp")
    columns = lax.axis_size("expert")
    local_experts = w_in.shape[0]
    experts = local_experts * columns
    token_count = hidden_in.shape[0]
    top_count = expert_ids.shape[1]
    capacity = max(2, token_count * top_count * 7 // (6 * experts))
    row_total = groups * token_count
    normed = normalize(hidden_in, norm_gain)
    model_width = hidden_in.shape[1]
    meta = jnp.concatenate([expert_ids.astype(jnp.bfloat16), gate_weights], axis=1)
    meta_row = jnp.zeros((1, model_width), jnp.bfloat16)
    meta_row = meta_row.at[0, : token_count * 2 * top_count].set(meta.reshape(-1))
    block = lax.all_gather(jnp.concatenate([normed, meta_row], axis=0), "dp", axis=0, tiled=False)
    gathered = block[:, :token_count].reshape(row_total, model_width)
    all_meta = block[:, token_count, : token_count * 2 * top_count].reshape(row_total, 2 * top_count)
    all_routes = all_meta[:, :top_count].astype(jnp.int32)
    all_gates = all_meta[:, top_count:]
    shared_width = shared_down.shape[0]
    shared_both = jnp.dot(gathered, shared_in, preferred_element_type=jnp.float32)
    shared_act = (
        jax.nn.silu(shared_both[:, :shared_width]) * shared_both[:, shared_width:]
    ).astype(jnp.bfloat16)
    shared_part = jnp.dot(shared_act, shared_down, preferred_element_type=jnp.float32).astype(
        jnp.bfloat16
    )
    slice_width = w_down.shape[1]

    def routes_of(routes, block_count):
        block_routes = routes.reshape(block_count, token_count * top_count)
        onehot = block_routes[:, :, None] == jnp.arange(experts, dtype=jnp.int32)[None, None, :]
        onehot_int = onehot.astype(jnp.int32)
        slot_rank = jnp.sum(jnp.cumsum(onehot_int, axis=1) * onehot_int, axis=2) - 1
        slot_of = jnp.sum(jnp.where(onehot, expert_slot[None, None, :], 0), axis=2)
        return slot_of // local_experts, slot_of % local_experts, slot_rank

    def expert_block(rows, local):
        gate_up = jnp.dot(rows, w_in[local], preferred_element_type=jnp.float32)
        activated = (
            jax.nn.silu(gate_up[:, :slice_width]) * gate_up[:, slice_width:]
        ).astype(jnp.bfloat16)
        return jnp.dot(activated, w_down[local], preferred_element_type=jnp.float32).astype(
            jnp.bfloat16
        )

    def one_hots(position, local_of, gates, local, buffer_rows):
        row_iota = jnp.arange(buffer_rows, dtype=jnp.int32)[None, None, :]
        hit = (position[:, :, None] == row_iota) & (local_of[:, :, None] == local)
        dispatch = jnp.any(hit, axis=1).astype(jnp.bfloat16)
        combine = jnp.sum(
            jnp.where(hit, gates[:, :, None], jnp.zeros((), jnp.bfloat16)), axis=1
        ).astype(jnp.bfloat16)
        return dispatch, combine

    dest_col, local_of, slot_rank = routes_of(all_routes, groups)
    group_of = jnp.arange(groups, dtype=jnp.int32)[:, None]
    position = ((dest_col * groups + group_of) * capacity + slot_rank).reshape(row_total, top_count)
    local_of = local_of.reshape(row_total, top_count)
    routed = shared_part.astype(jnp.float32)
    for local in range(local_experts - 1):
        dispatch, combine = one_hots(position, local_of, all_gates, local, columns * groups * capacity)
        outgoing = lax.dot_general(
            dispatch, gathered, (((0,), (0,)), ((), ())), preferred_element_type=jnp.float32
        ).astype(jnp.bfloat16)
        received = lax.all_to_all(outgoing, "expert", 0, 0, tiled=True)
        returned = lax.all_to_all(expert_block(received, local), "expert", 0, 0, tiled=True)
        routed = routed + jnp.dot(combine, returned, preferred_element_type=jnp.float32)
    last = local_experts - 1
    own_col, own_local, own_rank = routes_of(expert_ids, 1)
    own_position = (own_col * capacity + own_rank).reshape(token_count, top_count)
    own_local = own_local.reshape(token_count, top_count)
    dispatch, combine = one_hots(own_position, own_local, gate_weights, last, columns * capacity)
    outgoing = lax.dot_general(
        dispatch, normed, (((0,), (0,)), ((), ())), preferred_element_type=jnp.float32
    ).astype(jnp.bfloat16)
    received = lax.all_to_all(outgoing, "expert", 0, 0, tiled=True)
    spread = lax.all_gather(received, "dp", axis=0, tiled=True)
    summed = lax.psum_scatter(expert_block(spread, last), "dp", scatter_dimension=0, tiled=True)
    returned = lax.all_to_all(summed, "expert", 0, 0, tiled=True)
    own_routed = jnp.dot(combine, returned, preferred_element_type=jnp.float32)
    summed_rest = lax.psum_scatter(routed.astype(jnp.bfloat16), "dp", scatter_dimension=0, tiled=True)
    mixed = summed_rest.astype(jnp.float32) + own_routed
    return mixed.astype(jnp.bfloat16)


def solution(mesh):
    return jax.shard_map(
        on_device,
        mesh=mesh,
        in_specs=(
            P(("dp", "expert"), None),
            P(),
            P(("dp", "expert"), None),
            P(("dp", "expert"), None),
            P(),
            P("expert", None, "dp"),
            P("expert", "dp", None),
            P(None, "dp"),
            P("dp", None),
        ),
        out_specs=P(("dp", "expert"), None),
        check_vma=False,
    )
```

```python
import jax
import jax.numpy as jnp
from jax import lax
from jax.sharding import PartitionSpec as P

epsilon = 1e-06


def normalize(hidden, gain):
    widened = hidden.astype(jnp.float32)
    mean_square = jnp.mean(widened * widened, axis=-1, keepdims=True)
    return (widened * lax.rsqrt(mean_square + epsilon) * gain).astype(jnp.bfloat16)


def on_device(
    hidden_in,
    norm_gain,
    expert_ids,
    gate_weights,
    expert_slot,
    w_in,
    w_down,
    shared_in,
    shared_down,
):
    groups = lax.axis_size("dp")
    columns = lax.axis_size("expert")
    local_experts = w_in.shape[0]
    experts = local_experts * columns
    token_count = hidden_in.shape[0]
    top_count = expert_ids.shape[1]
    capacity = max(2, token_count * top_count * 7 // (6 * experts))
    row_total = groups * token_count
    normed = normalize(hidden_in, norm_gain)
    model_width = hidden_in.shape[1]
    def routes_of(routes, block_count):
        block_routes = routes.reshape(block_count, token_count * top_count)
        onehot = block_routes[:, :, None] == jnp.arange(experts, dtype=jnp.int32)[None, None, :]
        onehot_int = onehot.astype(jnp.int32)
        slot_rank = jnp.sum(jnp.cumsum(onehot_int, axis=1) * onehot_int, axis=2) - 1
        slot_of = jnp.sum(jnp.where(onehot, expert_slot[None, None, :], 0), axis=2)
        return slot_of, slot_rank

    own_slot, own_rank = routes_of(expert_ids, 1)
    own_slot = own_slot.reshape(token_count, top_count)
    own_rank = own_rank.reshape(token_count, top_count)
    meta = jnp.concatenate(
        [own_slot.astype(jnp.bfloat16), own_rank.astype(jnp.bfloat16), gate_weights], axis=1
    )
    meta_width = token_count * 3 * top_count
    meta_row = jnp.zeros((1, model_width), jnp.bfloat16)
    meta_row = meta_row.at[0, :meta_width].set(meta.reshape(-1))
    block = lax.all_gather(jnp.concatenate([normed, meta_row], axis=0), "dp", axis=0, tiled=False)
    gathered = block[:, :token_count].reshape(row_total, model_width)
    all_meta = block[:, token_count, :meta_width].reshape(row_total, 3 * top_count)
    all_slots = all_meta[:, :top_count].astype(jnp.int32)
    all_ranks = all_meta[:, top_count : 2 * top_count].astype(jnp.int32)
    all_gates = all_meta[:, 2 * top_count :]
    shared_width = shared_down.shape[0]
    shared_both = jnp.dot(gathered, shared_in, preferred_element_type=jnp.float32)
    shared_act = (
        jax.nn.silu(shared_both[:, :shared_width]) * shared_both[:, shared_width:]
    ).astype(jnp.bfloat16)
    shared_part = jnp.dot(shared_act, shared_down, preferred_element_type=jnp.float32).astype(
        jnp.bfloat16
    )
    slice_width = w_down.shape[1]

    def expert_block(rows, local):
        gate_up = jnp.dot(rows, w_in[local], preferred_element_type=jnp.float32)
        activated = (
            jax.nn.silu(gate_up[:, :slice_width]) * gate_up[:, slice_width:]
        ).astype(jnp.bfloat16)
        return jnp.dot(activated, w_down[local], preferred_element_type=jnp.float32).astype(
            jnp.bfloat16
        )

    def one_hots(position, local_of, gates, local, buffer_rows):
        row_iota = jnp.arange(buffer_rows, dtype=jnp.int32)[None, None, :]
        hit = (position[:, :, None] == row_iota) & (local_of[:, :, None] == local)
        dispatch = jnp.any(hit, axis=1).astype(jnp.bfloat16)
        combine = jnp.sum(
            jnp.where(hit, gates[:, :, None], jnp.zeros((), jnp.bfloat16)), axis=1
        ).astype(jnp.bfloat16)
        return dispatch, combine

    group_of = (jnp.arange(row_total, dtype=jnp.int32) // token_count)[:, None]
    position = ((all_slots // local_experts) * groups + group_of) * capacity + all_ranks
    local_of = all_slots % local_experts
    routed = shared_part.astype(jnp.float32)
    for local in range(local_experts - 1):
        dispatch, combine = one_hots(position, local_of, all_gates, local, columns * groups * capacity)
        outgoing = lax.dot_general(
            dispatch, gathered, (((0,), (0,)), ((), ())), preferred_element_type=jnp.float32
        ).astype(jnp.bfloat16)
        received = lax.all_to_all(outgoing, "expert", 0, 0, tiled=True)
        returned = lax.all_to_all(expert_block(received, local), "expert", 0, 0, tiled=True)
        routed = routed + jnp.dot(combine, returned, preferred_element_type=jnp.float32)
    last = local_experts - 1
    own_position = (own_slot // local_experts) * capacity + own_rank
    own_local = own_slot % local_experts
    dispatch, combine = one_hots(own_position, own_local, gate_weights, last, columns * capacity)
    outgoing = lax.dot_general(
        dispatch, normed, (((0,), (0,)), ((), ())), preferred_element_type=jnp.float32
    ).astype(jnp.bfloat16)
    received = lax.all_to_all(outgoing, "expert", 0, 0, tiled=True)
    spread = lax.all_gather(received, "dp", axis=0, tiled=True)
    summed = lax.psum_scatter(expert_block(spread, last), "dp", scatter_dimension=0, tiled=True)
    returned = lax.all_to_all(summed, "expert", 0, 0, tiled=True)
    own_routed = jnp.dot(combine, returned, preferred_element_type=jnp.float32)
    summed_rest = lax.psum_scatter(routed.astype(jnp.bfloat16), "dp", scatter_dimension=0, tiled=True)
    mixed = summed_rest.astype(jnp.float32) + own_routed
    return mixed.astype(jnp.bfloat16)


def solution(mesh):
    return jax.shard_map(
        on_device,
        mesh=mesh,
        in_specs=(
            P(("dp", "expert"), None),
            P(),
            P(("dp", "expert"), None),
            P(("dp", "expert"), None),
            P(),
            P("expert", None, "dp"),
            P("expert", "dp", None),
            P(None, "dp"),
            P("dp", None),
        ),
        out_specs=P(("dp", "expert"), None),
        check_vma=False,
    )
```

```python
import jax
import jax.numpy as jnp
from jax import lax
from jax.sharding import PartitionSpec as P

epsilon = 1e-06


def normalize(hidden, gain):
    widened = hidden.astype(jnp.float32)
    mean_square = jnp.mean(widened * widened, axis=-1, keepdims=True)
    return (widened * lax.rsqrt(mean_square + epsilon) * gain).astype(jnp.bfloat16)


def on_device(
    hidden_in,
    norm_gain,
    expert_ids,
    gate_weights,
    expert_slot,
    w_in,
    w_down,
    shared_in,
    shared_down,
):
    groups = lax.axis_size("dp")
    columns = lax.axis_size("expert")
    local_experts = w_in.shape[0]
    experts = local_experts * columns
    token_count = hidden_in.shape[0]
    top_count = expert_ids.shape[1]
    capacity = max(2, token_count * top_count * 7 // (6 * experts))
    row_total = groups * token_count
    normed = normalize(hidden_in, norm_gain)
    model_width = hidden_in.shape[1]
    def routes_of(routes, block_count):
        block_routes = routes.reshape(block_count, token_count * top_count)
        onehot = block_routes[:, :, None] == jnp.arange(experts, dtype=jnp.int32)[None, None, :]
        onehot_int = onehot.astype(jnp.int32)
        slot_rank = jnp.sum(jnp.cumsum(onehot_int, axis=1) * onehot_int, axis=2) - 1
        slot_of = jnp.sum(jnp.where(onehot, expert_slot[None, None, :], 0), axis=2)
        return slot_of, slot_rank

    own_slot, own_rank = routes_of(expert_ids, 1)
    own_slot = own_slot.reshape(token_count, top_count)
    own_rank = own_rank.reshape(token_count, top_count)
    meta = jnp.concatenate(
        [own_slot.astype(jnp.bfloat16), own_rank.astype(jnp.bfloat16), gate_weights], axis=1
    )
    meta_width = token_count * 3 * top_count
    meta_row = jnp.zeros((1, model_width), jnp.bfloat16)
    meta_row = meta_row.at[0, :meta_width].set(meta.reshape(-1))
    block = lax.all_gather(jnp.concatenate([normed, meta_row], axis=0), "dp", axis=0, tiled=False)
    gathered = block[:, :token_count].reshape(row_total, model_width)
    all_meta = block[:, token_count, :meta_width].reshape(row_total, 3 * top_count)
    all_slots = all_meta[:, :top_count].astype(jnp.int32)
    all_ranks = all_meta[:, top_count : 2 * top_count].astype(jnp.int32)
    all_gates = all_meta[:, 2 * top_count :]
    shared_width = shared_down.shape[0]
    shared_both = jnp.dot(gathered, shared_in, preferred_element_type=jnp.float32)
    shared_act = (
        jax.nn.silu(shared_both[:, :shared_width]) * shared_both[:, shared_width:]
    ).astype(jnp.bfloat16)
    shared_part = jnp.dot(shared_act, shared_down, preferred_element_type=jnp.float32).astype(
        jnp.bfloat16
    )
    slice_width = w_down.shape[1]

    def expert_block(rows, local):
        gate_up = jnp.dot(rows, w_in[local], preferred_element_type=jnp.float32)
        activated = (
            jax.nn.silu(gate_up[:, :slice_width]) * gate_up[:, slice_width:]
        ).astype(jnp.bfloat16)
        return jnp.dot(activated, w_down[local], preferred_element_type=jnp.float32).astype(
            jnp.bfloat16
        )

    def one_hots(position, local_of, gates, local, buffer_rows):
        row_iota = jnp.arange(buffer_rows, dtype=jnp.int32)[None, None, :]
        hit = (position[:, :, None] == row_iota) & (local_of[:, :, None] == local)
        dispatch = jnp.any(hit, axis=1).astype(jnp.bfloat16)
        combine = jnp.sum(
            jnp.where(hit, gates[:, :, None], jnp.zeros((), jnp.bfloat16)), axis=1
        ).astype(jnp.bfloat16)
        return dispatch, combine

    group_of = (jnp.arange(row_total, dtype=jnp.int32) // token_count)[:, None]
    position = ((all_slots // local_experts) * groups + group_of) * capacity + all_ranks
    local_of = all_slots % local_experts
    halves = 2
    half_width = model_width // halves
    summed_parts = []
    for local in range(local_experts - 1):
        dispatch, combine = one_hots(position, local_of, all_gates, local, columns * groups * capacity)
        outgoing = lax.dot_general(
            dispatch, gathered, (((0,), (0,)), ((), ())), preferred_element_type=jnp.float32
        ).astype(jnp.bfloat16)
        received = lax.all_to_all(outgoing, "expert", 0, 0, tiled=True)
        gate_up = jnp.dot(received, w_in[local], preferred_element_type=jnp.float32)
        activated = (
            jax.nn.silu(gate_up[:, :slice_width]) * gate_up[:, slice_width:]
        ).astype(jnp.bfloat16)
        for half in range(halves):
            cols = slice(half * half_width, (half + 1) * half_width)
            partial_value = jnp.dot(
                activated, w_down[local][:, cols], preferred_element_type=jnp.float32
            ).astype(jnp.bfloat16)
            returned = lax.all_to_all(partial_value, "expert", 0, 0, tiled=True)
            routed = shared_part[:, cols].astype(jnp.float32) + jnp.dot(
                combine, returned, preferred_element_type=jnp.float32
            )
            summed_parts.append(
                lax.psum_scatter(routed.astype(jnp.bfloat16), "dp", scatter_dimension=0, tiled=True)
            )
    last = local_experts - 1
    own_position = (own_slot // local_experts) * capacity + own_rank
    own_local = own_slot % local_experts
    dispatch, combine = one_hots(own_position, own_local, gate_weights, last, columns * capacity)
    outgoing = lax.dot_general(
        dispatch, normed, (((0,), (0,)), ((), ())), preferred_element_type=jnp.float32
    ).astype(jnp.bfloat16)
    received = lax.all_to_all(outgoing, "expert", 0, 0, tiled=True)
    spread = lax.all_gather(received, "dp", axis=0, tiled=True)
    summed = lax.psum_scatter(expert_block(spread, last), "dp", scatter_dimension=0, tiled=True)
    returned = lax.all_to_all(summed, "expert", 0, 0, tiled=True)
    own_routed = jnp.dot(combine, returned, preferred_element_type=jnp.float32)
    summed_rest = jnp.concatenate(summed_parts, axis=1)
    mixed = summed_rest.astype(jnp.float32) + own_routed
    return mixed.astype(jnp.bfloat16)


def solution(mesh):
    return jax.shard_map(
        on_device,
        mesh=mesh,
        in_specs=(
            P(("dp", "expert"), None),
            P(),
            P(("dp", "expert"), None),
            P(("dp", "expert"), None),
            P(),
            P("expert", None, "dp"),
            P("expert", "dp", None),
            P(None, "dp"),
            P("dp", None),
        ),
        out_specs=P(("dp", "expert"), None),
        check_vma=False,
    )
```

```python
import jax
import jax.numpy as jnp
from jax import lax
from jax.sharding import PartitionSpec as P

epsilon = 1e-06


def normalize(hidden, gain):
    widened = hidden.astype(jnp.float32)
    mean_square = jnp.mean(widened * widened, axis=-1, keepdims=True)
    return (widened * lax.rsqrt(mean_square + epsilon) * gain).astype(jnp.bfloat16)


def on_device(
    hidden_in,
    norm_gain,
    expert_ids,
    gate_weights,
    expert_slot,
    w_in,
    w_down,
    shared_in,
    shared_down,
):
    groups = lax.axis_size("dp")
    columns = lax.axis_size("expert")
    local_experts = w_in.shape[0]
    experts = local_experts * columns
    token_count = hidden_in.shape[0]
    top_count = expert_ids.shape[1]
    capacity = max(2, token_count * top_count * 7 // (6 * experts))
    row_total = groups * token_count
    normed = normalize(hidden_in, norm_gain)
    model_width = hidden_in.shape[1]
    def routes_of(routes, block_count):
        block_routes = routes.reshape(block_count, token_count * top_count)
        onehot = block_routes[:, :, None] == jnp.arange(experts, dtype=jnp.int32)[None, None, :]
        onehot_int = onehot.astype(jnp.int32)
        slot_rank = jnp.sum(jnp.cumsum(onehot_int, axis=1) * onehot_int, axis=2) - 1
        slot_of = jnp.sum(jnp.where(onehot, expert_slot[None, None, :], 0), axis=2)
        return slot_of, slot_rank

    own_slot, own_rank = routes_of(expert_ids, 1)
    own_slot = own_slot.reshape(token_count, top_count)
    own_rank = own_rank.reshape(token_count, top_count)
    meta = jnp.concatenate(
        [own_slot.astype(jnp.bfloat16), own_rank.astype(jnp.bfloat16), gate_weights], axis=1
    )
    meta_width = token_count * 3 * top_count
    meta_row = jnp.zeros((1, model_width), jnp.bfloat16)
    meta_row = meta_row.at[0, :meta_width].set(meta.reshape(-1))
    block = lax.all_gather(jnp.concatenate([normed, meta_row], axis=0), "dp", axis=0, tiled=False)
    gathered = block[:, :token_count].reshape(row_total, model_width)
    all_meta = block[:, token_count, :meta_width].reshape(row_total, 3 * top_count)
    all_slots = all_meta[:, :top_count].astype(jnp.int32)
    all_ranks = all_meta[:, top_count : 2 * top_count].astype(jnp.int32)
    all_gates = all_meta[:, 2 * top_count :]
    shared_width = shared_down.shape[0]
    shared_both = jnp.dot(gathered, shared_in, preferred_element_type=jnp.float32)
    shared_act = (
        jax.nn.silu(shared_both[:, :shared_width]) * shared_both[:, shared_width:]
    ).astype(jnp.bfloat16)
    shared_part = jnp.dot(shared_act, shared_down, preferred_element_type=jnp.float32).astype(
        jnp.bfloat16
    )
    slice_width = w_down.shape[1]

    def expert_block(rows, local):
        gate_up = jnp.dot(rows, w_in[local], preferred_element_type=jnp.float32)
        activated = (
            jax.nn.silu(gate_up[:, :slice_width]) * gate_up[:, slice_width:]
        ).astype(jnp.bfloat16)
        return jnp.dot(activated, w_down[local], preferred_element_type=jnp.float32).astype(
            jnp.bfloat16
        )

    def one_hots(position, local_of, gates, local, buffer_rows):
        row_iota = jnp.arange(buffer_rows, dtype=jnp.int32)[None, None, :]
        hit = (position[:, :, None] == row_iota) & (local_of[:, :, None] == local)
        dispatch = jnp.any(hit, axis=1).astype(jnp.bfloat16)
        combine = jnp.sum(
            jnp.where(hit, gates[:, :, None], jnp.zeros((), jnp.bfloat16)), axis=1
        ).astype(jnp.bfloat16)
        return dispatch, combine

    group_of = (jnp.arange(row_total, dtype=jnp.int32) // token_count)[:, None]
    position = ((all_slots // local_experts) * groups + group_of) * capacity + all_ranks
    local_of = all_slots % local_experts
    routed = shared_part.astype(jnp.float32)
    for local in range(local_experts - 1):
        dispatch, combine = one_hots(position, local_of, all_gates, local, columns * groups * capacity)
        outgoing = lax.dot_general(
            dispatch, gathered, (((0,), (0,)), ((), ())), preferred_element_type=jnp.float32
        ).astype(jnp.bfloat16)
        received = lax.all_to_all(outgoing, "expert", 0, 0, tiled=True)
        returned = lax.all_to_all(expert_block(received, local), "expert", 0, 0, tiled=True)
        combined, combine_a, returned_a = routed, combine, returned
    last = local_experts - 1
    own_position = (own_slot // local_experts) * capacity + own_rank
    own_local = own_slot % local_experts
    dispatch, combine = one_hots(own_position, own_local, gate_weights, last, columns * capacity)
    outgoing = lax.dot_general(
        dispatch, normed, (((0,), (0,)), ((), ())), preferred_element_type=jnp.float32
    ).astype(jnp.bfloat16)
    received = lax.all_to_all(outgoing, "expert", 0, 0, tiled=True)
    spread = lax.all_gather(received, "dp", axis=0, tiled=True)
    summed = lax.psum_scatter(expert_block(spread, last), "dp", scatter_dimension=0, tiled=True)
    returned = lax.all_to_all(summed, "expert", 0, 0, tiled=True)
    own_routed = jnp.dot(combine, returned, preferred_element_type=jnp.float32)
    half_width = model_width // 2
    summed_parts = []
    for half in range(2):
        cols = slice(half * half_width, (half + 1) * half_width)
        part = combined[:, cols] + jnp.dot(
            combine_a, returned_a[:, cols], preferred_element_type=jnp.float32
        )
        summed_parts.append(
            lax.psum_scatter(part.astype(jnp.bfloat16), "dp", scatter_dimension=0, tiled=True)
        )
    summed_rest = jnp.concatenate(summed_parts, axis=1)
    mixed = summed_rest.astype(jnp.float32) + own_routed
    return mixed.astype(jnp.bfloat16)


def solution(mesh):
    return jax.shard_map(
        on_device,
        mesh=mesh,
        in_specs=(
            P(("dp", "expert"), None),
            P(),
            P(("dp", "expert"), None),
            P(("dp", "expert"), None),
            P(),
            P("expert", None, "dp"),
            P("expert", "dp", None),
            P(None, "dp"),
            P("dp", None),
        ),
        out_specs=P(("dp", "expert"), None),
        check_vma=False,
    )
```
